32 devices in a mesh: led: 4 (over y, x), row: 8 (over z, core).
Axes of the slice: x: 2, y: 2, z: 4, core: 2. Of those that a mesh axis runs over, the one named last changes fastest.
Arguments:
- spectrum: float32 [2, 4096, 4096], P(None, 'led', 'row'), may hold values from -6 to 6
- amplitudes: float32 [4, 2048, 2048], P('led', 'row'), may hold values from 0.2 to 3
- offsets: int32 [4, 2], replicated, may hold values from 0 to 2048
- coeffs: float32 [6], replicated, may hold values from -2.5 to 2.5
Outputs:
- updated: float32 [2, 4096, 4096], P(None, 'led', 'row')
The draws below stay inside these ranges and needn't reach their ends.
All inputs are finite; a program needn't handle non-finite values.
Results may differ from the reference program's by a relative error of at most 0.0001.
Values sent between devices are 32-bit elements; how exact they have to be, the bound alone decides.
No kernel may reach another device: no remote copies, remote signals or barrier semaphores. Data moves between devices by JAX's collectives and lax.ppermute only.
A program may use at most 128 MiB of HBM per device.

```python
import math
import jax
import jax.numpy as jnp
from jax import lax

M = 2048
S = 4096
TERMS = 6
LEDS = 4


def set_ends(entries, stream_key, smallest, top_value):
    spot = [jax.random.randint(jax.random.fold_in(stream_key, axis), (), 0, length) for axis, length in enumerate(entries.shape)]
    longest = entries.shape.index(max(entries.shape))
    beside = spot[:longest] + [(spot[longest] + 1) % entries.shape[longest]] + spot[longest + 1:]
    return entries.at[tuple(spot)].set(smallest).at[tuple(beside)].set(top_value)


def level_of(stream_key, dims, pieces, smallest, largest):
    loudness = 1.0
    for position, blocks in pieces:
        heights = jax.random.uniform(jax.random.fold_in(jax.random.fold_in(stream_key, 6), position), (blocks,), jnp.float32, smallest / len(pieces), largest / len(pieces))
        loudness = loudness * jnp.repeat(jnp.exp(heights), dims[position] // blocks).reshape((-1,) + (1,) * (len(dims) - 1 - position))
    return loudness


def normal_values(stream_key, shape, spread, reach, split=(), kind=jnp.bfloat16):
    drawn = jax.random.normal(stream_key, shape, jnp.float32) * spread
    if len(split) > 0:
        drawn = level_of(stream_key, shape, split, -0.22, 0.18) * drawn
    return jnp.clip(drawn, min=-reach, max=reach).astype(kind)


def setup_inputs(seed: int = 0) -> dict:
    streams_of = jax.random.split(jax.random.key(seed), 5)
    return {
        "spectrum": normal_values(streams_of[0], (2, S, S), 1.0, 6.0, ((1, 4), (2, 8)), jnp.float32),
        "amplitudes": jnp.clip(jnp.exp(math.log(3.0) - 2.7080502 * jax.random.uniform(streams_of[1], (LEDS, M, M), jnp.float32) ** level_of(streams_of[1], (LEDS, M, M), ((0, 4), (1, 8)), -0.2, 0.2)), 0.2, 3.0),
        "offsets": set_ends(jax.random.randint(streams_of[2], (LEDS, 2), 0, S - M + 1), jax.random.fold_in(streams_of[2], 1), 0, S - M).astype(jnp.int32),
        "coeffs": normal_values(streams_of[3], (TERMS,), 0.8, 2.5, (), jnp.float32),
    }


SOFTENING = 0.1

def pupil_at(down_index, across_index, coeffs, centre):
    offset_down = down_index - centre
    offset_across = across_index - centre
    inside = offset_down * offset_down + offset_across * offset_across < centre * centre
    upper_norm = offset_down.astype(jnp.float32) * (1.0 / centre)
    lateral = offset_across.astype(jnp.float32) * (1.0 / centre)
    radial = upper_norm * upper_norm + lateral * lateral
    phases = coeffs[0] * (2.0 * radial - 1.0) + coeffs[1] * (upper_norm * upper_norm - lateral * lateral) + coeffs[2] * (2.0 * upper_norm * lateral) + (3.0 * radial - 2.0) * (coeffs[3] * upper_norm + coeffs[4] * lateral) + coeffs[5] * (6.0 * radial * radial - 6.0 * radial + 1.0)
    weight = jnp.where(inside, 1.0, 0.0).astype(jnp.float32)
    return (weight * jnp.cos(phases), weight * jnp.sin(phases))

def reference(spectrum, amplitudes, offsets, coeffs):
    indices = jnp.arange(M, dtype=jnp.int32)
    pupil_re, pupil_im = pupil_at(indices[:, None], indices[None, :], coeffs, M // 2)
    pupil_field = lax.complex(pupil_re, pupil_im)
    region = lax.complex(spectrum[0], spectrum[1])
    accumulated = jnp.zeros_like(region)
    for source in range(LEDS):
        corner = (offsets[source, 0].astype(jnp.int32), offsets[source, 1].astype(jnp.int32))
        window = lax.dynamic_slice(region, corner, (M, M))
        field_now = jnp.fft.ifft2(pupil_field * window, norm='ortho')
        magnitude = jnp.sqrt(field_now.real * field_now.real + field_now.imag * field_now.imag + SOFTENING)
        difference = field_now * (amplitudes[source] / magnitude) - field_now
        update = jnp.conj(pupil_field) * jnp.fft.fft2(difference, norm='ortho')
        current = lax.dynamic_slice(accumulated, corner, (M, M))
        accumulated = lax.dynamic_update_slice(accumulated, current + update, corner)
    return jnp.stack([spectrum[0] + accumulated.real, spectrum[1] + accumulated.imag])
```

```python
import math

import jax
import jax.numpy as jnp
from jax import lax
from jax.sharding import PartitionSpec as P

SOFTENING = 0.1
HIGHEST_PRECISION = lax.Precision.HIGHEST
CHUNKS = 2


def pupil_at(down_index, across_index, coeffs, centre):
    offset_down = down_index - centre
    offset_across = across_index - centre
    inside = offset_down * offset_down + offset_across * offset_across < centre * centre
    upper_norm = offset_down.astype(jnp.float32) * (1.0 / centre)
    lateral = offset_across.astype(jnp.float32) * (1.0 / centre)
    radial = upper_norm * upper_norm + lateral * lateral
    phases = (
        coeffs[0] * (2.0 * radial - 1.0)
        + coeffs[1] * (upper_norm * upper_norm - lateral * lateral)
        + coeffs[2] * (2.0 * upper_norm * lateral)
        + (3.0 * radial - 2.0) * (coeffs[3] * upper_norm + coeffs[4] * lateral)
        + coeffs[5] * (6.0 * radial * radial - 6.0 * radial + 1.0)
    )
    weight = jnp.where(inside, 1.0, 0.0).astype(jnp.float32)
    return (weight * jnp.cos(phases), weight * jnp.sin(phases))


def tables(outer_size, inner_size, direction):
    length = outer_size * inner_size
    angle_step = direction * 2.0 * math.pi / length
    first_index = jnp.arange(outer_size, dtype=jnp.int32)
    grid_first = first_index[:, None] * first_index[None, :] * inner_size % length
    angles_first = grid_first.astype(jnp.float32) * angle_step
    index_k = jnp.arange(outer_size, dtype=jnp.int32)[:, None, None]
    index_r = jnp.arange(inner_size, dtype=jnp.int32)[None, :, None]
    index_j = jnp.arange(inner_size, dtype=jnp.int32)[None, None, :]
    grid_second = index_r * (index_k + outer_size * index_j) % length
    angles_second = grid_second.astype(jnp.float32) * angle_step
    return (
        jnp.cos(angles_first),
        jnp.sin(angles_first),
        jnp.cos(angles_second),
        jnp.sin(angles_second),
    )


def transform(paired, inputs, middle, output, outer_size, inner_size, direction):
    first_re, first_im, second_re, second_im = tables(outer_size, inner_size, direction)
    scaling = 1.0 / math.sqrt(outer_size * inner_size)
    first_table = jnp.stack([jnp.stack([first_re, first_im]), jnp.stack([-first_im, first_re])])
    second_table = (
        jnp.stack([jnp.stack([second_re, second_im]), jnp.stack([-second_im, second_re])]) * scaling
    )
    middle_pair = jnp.einsum(
        "p" + inputs + ",pqtk->q" + middle, paired, first_table, precision=HIGHEST_PRECISION
    )
    return jnp.einsum(
        "p" + middle + ",pqkrj->q" + output, middle_pair, second_table, precision=HIGHEST_PRECISION
    )


def unit_times(value_re, value_im, turn):
    eighths = round(turn * 8) % 8
    if eighths == 0:
        return value_re, value_im
    if eighths == 2:
        return -value_im, value_re
    if eighths == 4:
        return -value_re, -value_im
    if eighths == 6:
        return value_im, -value_re
    c = math.cos(2.0 * math.pi * turn)
    s = math.sin(2.0 * math.pi * turn)
    return value_re * c - value_im * s, value_re * s + value_im * c


def row_transform(pair_re, pair_im, direction, inner=4):
    length, width = pair_re.shape
    outer = length // inner
    angle_step = direction * 2.0 * math.pi / outer
    index = jnp.arange(outer, dtype=jnp.int32)
    grid = (index[:, None] * index[None, :]) % outer
    angles = grid.astype(jnp.float32) * angle_step
    cos_t = jnp.cos(angles)
    sin_t = jnp.sin(angles)
    table = jnp.concatenate(
        [jnp.concatenate([cos_t, -sin_t], axis=1), jnp.concatenate([sin_t, cos_t], axis=1)], axis=0
    )
    stacked = jnp.concatenate(
        [pair_re.reshape(outer, inner * width), pair_im.reshape(outer, inner * width)], axis=0
    )
    middle = jnp.dot(table, stacked, precision=HIGHEST_PRECISION)
    mid_re = middle[:outer]
    mid_im = middle[outer:]
    scaling = 1.0 / math.sqrt(length)
    twiddled = []
    for r in range(inner):
        part_re = mid_re[:, r * width:(r + 1) * width]
        part_im = mid_im[:, r * width:(r + 1) * width]
        if r == 0:
            twiddled.append((part_re * scaling, part_im * scaling))
            continue
        tw_angle = (r * index % length).astype(jnp.float32) * (direction * 2.0 * math.pi / length)
        tw_re = (jnp.cos(tw_angle) * scaling)[:, None]
        tw_im = (jnp.sin(tw_angle) * scaling)[:, None]
        twiddled.append((part_re * tw_re - part_im * tw_im, part_re * tw_im + part_im * tw_re))
    out_re = []
    out_im = []
    for j in range(inner):
        acc_re = None
        acc_im = None
        for r in range(inner):
            t_re, t_im = unit_times(twiddled[r][0], twiddled[r][1], direction * r * j / inner)
            acc_re = t_re if acc_re is None else acc_re + t_re
            acc_im = t_im if acc_im is None else acc_im + t_im
        out_re.append(acc_re)
        out_im.append(acc_im)
    return jnp.concatenate(out_re, axis=0), jnp.concatenate(out_im, axis=0)


def correct(field_re, field_im, measured):
    magnitude = jnp.sqrt(field_re * field_re + field_im * field_im + SOFTENING)
    factor = measured / magnitude
    return (field_re * factor - field_re, field_im * factor - field_im)


def on_device(spectrum, amplitudes, offsets, coeffs):
    led_count = lax.axis_size("led")
    row_count = lax.axis_size("row")
    led_index = lax.axis_index("led")
    row_index = lax.axis_index("row")
    size_rows = spectrum.shape[1]
    size_cols = spectrum.shape[2]
    window = amplitudes.shape[2]
    centre = window // 2
    block_rows = window // row_count
    outer_cols = window // row_count
    chunks = max(1, min(CHUNKS, size_cols // 128))
    width = size_cols // chunks
    row_shift = offsets[led_index, 0]
    col_shift = offsets[led_index, 1]
    measured = amplitudes[0]
    shape_cols = (2, block_rows, outer_cols, row_count)
    row_ids = jnp.arange(window, dtype=jnp.int32)[:, None]

    pupils = []
    spreads = []
    for chunk in range(chunks):
        part = spectrum[:, :, chunk * width:(chunk + 1) * width]
        region = lax.all_gather(part, "led", axis=1, tiled=True)
        band = lax.dynamic_slice_in_dim(region, row_shift, window, 1)
        col_ids = (
            row_index * size_cols + chunk * width + jnp.arange(width, dtype=jnp.int32)
        )[None, :] - col_shift
        pupil_re, pupil_im = pupil_at(row_ids, col_ids, coeffs, centre)
        pupils.append((pupil_re, pupil_im))
        lit_re = pupil_re * band[0] - pupil_im * band[1]
        lit_im = pupil_re * band[1] + pupil_im * band[0]
        half_re, half_im = row_transform(lit_re, lit_im, 1.0)
        stacked = jnp.stack([half_re, half_im])
        spread = lax.all_to_all(stacked, "row", split_axis=1, concat_axis=2, tiled=True)
        spreads.append(spread.reshape(2, block_rows, row_count, width))
    spread_all = jnp.stack(spreads, axis=3).reshape(2, block_rows, row_count * size_cols)
    window_part = lax.dynamic_slice_in_dim(spread_all, col_shift, window, 2)
    field = transform(
        window_part.reshape(shape_cols), "ytr", "ykr", "yjk", outer_cols, row_count, 1.0
    )
    field = field.reshape(2, block_rows, window)
    diff_re, diff_im = correct(field[0], field[1], measured)
    back = transform(
        jnp.stack([diff_re, diff_im]).reshape(shape_cols),
        "ytr",
        "ykr",
        "yjk",
        outer_cols,
        row_count,
        -1.0,
    )
    padded = jnp.zeros((2, block_rows, row_count * size_cols), jnp.float32)
    padded = lax.dynamic_update_slice_in_dim(
        padded, back.reshape(2, block_rows, window), col_shift, 2
    )
    padded = padded.reshape(2, block_rows, row_count, chunks, width)
    results = []
    for chunk in range(chunks):
        piece = padded[:, :, :, chunk, :].reshape(2, block_rows, row_count * width)
        gathered = lax.all_to_all(piece, "row", split_axis=2, concat_axis=1, tiled=True)
        spec_re, spec_im = row_transform(gathered[0], gathered[1], -1.0)
        pupil_re, pupil_im = pupils[chunk]
        upd_re = pupil_re * spec_re + pupil_im * spec_im
        upd_im = pupil_re * spec_im - pupil_im * spec_re
        embedded = jnp.zeros((2, size_rows * led_count, width), jnp.float32)
        embedded = lax.dynamic_update_slice_in_dim(
            embedded, jnp.stack([upd_re, upd_im]), row_shift, 1
        )
        results.append(lax.psum_scatter(embedded, "led", scatter_dimension=1, tiled=True))
    summed = jnp.concatenate(results, axis=2)
    return spectrum + summed


def solution(mesh):
    return jax.shard_map(
        on_device,
        mesh=mesh,
        in_specs=(P(None, "led", "row"), P("led", "row", None), P(), P()),
        out_specs=P(None, "led", "row"),
        check_vma=False,
    )
```

```python
import math

import jax
import jax.numpy as jnp
from jax import lax
from jax.sharding import PartitionSpec as P


SOFTENING = 0.1
HIGHEST_PRECISION = lax.Precision.HIGH
CHUNKS = 4


def pupil_at(down_index, across_index, coeffs, centre):
    offset_down = down_index - centre
    offset_across = across_index - centre
    inside = offset_down * offset_down + offset_across * offset_across < centre * centre
    upper_norm = offset_down.astype(jnp.float32) * (1.0 / centre)
    lateral = offset_across.astype(jnp.float32) * (1.0 / centre)
    radial = upper_norm * upper_norm + lateral * lateral
    phases = (
        coeffs[0] * (2.0 * radial - 1.0)
        + coeffs[1] * (upper_norm * upper_norm - lateral * lateral)
        + coeffs[2] * (2.0 * upper_norm * lateral)
        + (3.0 * radial - 2.0) * (coeffs[3] * upper_norm + coeffs[4] * lateral)
        + coeffs[5] * (6.0 * radial * radial - 6.0 * radial + 1.0)
    )
    weight = jnp.where(inside, 1.0, 0.0).astype(jnp.float32)
    return (weight * jnp.cos(phases), weight * jnp.sin(phases))


def tables(outer_size, inner_size, direction):
    length = outer_size * inner_size
    angle_step = direction * 2.0 * math.pi / length
    first_index = jnp.arange(outer_size, dtype=jnp.int32)
    grid_first = first_index[:, None] * first_index[None, :] * inner_size % length
    angles_first = grid_first.astype(jnp.float32) * angle_step
    index_k = jnp.arange(outer_size, dtype=jnp.int32)[:, None, None]
    index_r = jnp.arange(inner_size, dtype=jnp.int32)[None, :, None]
    index_j = jnp.arange(inner_size, dtype=jnp.int32)[None, None, :]
    grid_second = index_r * (index_k + outer_size * index_j) % length
    angles_second = grid_second.astype(jnp.float32) * angle_step
    return (
        jnp.cos(angles_first),
        jnp.sin(angles_first),
        jnp.cos(angles_second),
        jnp.sin(angles_second),
    )


def transform(paired, inputs, middle, output, outer_size, inner_size, direction):
    first_re, first_im, second_re, second_im = tables(outer_size, inner_size, direction)
    scaling = 1.0 / math.sqrt(outer_size * inner_size)
    first_table = jnp.stack([jnp.stack([first_re, first_im]), jnp.stack([-first_im, first_re])])
    second_table = (
        jnp.stack([jnp.stack([second_re, second_im]), jnp.stack([-second_im, second_re])]) * scaling
    )
    middle_pair = jnp.einsum(
        "p" + inputs + ",pqtk->q" + middle, paired, first_table, precision=HIGHEST_PRECISION
    )
    return jnp.einsum(
        "p" + middle + ",pqkrj->q" + output, middle_pair, second_table, precision=HIGHEST_PRECISION
    )


def unit_times(value_re, value_im, turn):
    eighths = round(turn * 8) % 8
    if eighths == 0:
        return value_re, value_im
    if eighths == 2:
        return -value_im, value_re
    if eighths == 4:
        return -value_re, -value_im
    if eighths == 6:
        return value_im, -value_re
    c = math.cos(2.0 * math.pi * turn)
    s = math.sin(2.0 * math.pi * turn)
    return value_re * c - value_im * s, value_re * s + value_im * c


def row_transform(pair_re, pair_im, direction, inner=4):
    length, width = pair_re.shape
    outer = length // inner
    angle_step = direction * 2.0 * math.pi / outer
    index = jnp.arange(outer, dtype=jnp.int32)
    grid = (index[:, None] * index[None, :]) % outer
    angles = grid.astype(jnp.float32) * angle_step
    cos_t = jnp.cos(angles)
    sin_t = jnp.sin(angles)
    table = jnp.concatenate(
        [jnp.concatenate([cos_t, -sin_t], axis=1), jnp.concatenate([sin_t, cos_t], axis=1)], axis=0
    )
    stacked = jnp.concatenate(
        [pair_re.reshape(outer, inner * width), pair_im.reshape(outer, inner * width)], axis=0
    )
    middle = jnp.dot(table, stacked, precision=HIGHEST_PRECISION)
    mid_re = middle[:outer]
    mid_im = middle[outer:]
    scaling = 1.0 / math.sqrt(length)
    twiddled = []
    for r in range(inner):
        part_re = mid_re[:, r * width:(r + 1) * width]
        part_im = mid_im[:, r * width:(r + 1) * width]
        if r == 0:
            twiddled.append((part_re * scaling, part_im * scaling))
            continue
        tw_angle = (r * index % length).astype(jnp.float32) * (direction * 2.0 * math.pi / length)
        tw_re = (jnp.cos(tw_angle) * scaling)[:, None]
        tw_im = (jnp.sin(tw_angle) * scaling)[:, None]
        twiddled.append((part_re * tw_re - part_im * tw_im, part_re * tw_im + part_im * tw_re))
    out_re = []
    out_im = []
    for j in range(inner):
        acc_re = None
        acc_im = None
        for r in range(inner):
            t_re, t_im = unit_times(twiddled[r][0], twiddled[r][1], direction * r * j / inner)
            acc_re = t_re if acc_re is None else acc_re + t_re
            acc_im = t_im if acc_im is None else acc_im + t_im
        out_re.append(acc_re)
        out_im.append(acc_im)
    return jnp.concatenate(out_re, axis=0), jnp.concatenate(out_im, axis=0)


def correct(field_re, field_im, measured):
    magnitude = jnp.sqrt(field_re * field_re + field_im * field_im + SOFTENING)
    factor = measured / magnitude
    return (field_re * factor - field_re, field_im * factor - field_im)


def on_device(spectrum, amplitudes, offsets, coeffs):
    led_count = lax.axis_size("led")
    row_count = lax.axis_size("row")
    led_index = lax.axis_index("led")
    row_index = lax.axis_index("row")
    size_rows = spectrum.shape[1]
    size_cols = spectrum.shape[2]
    window = amplitudes.shape[2]
    centre = window // 2
    block_rows = window // row_count
    outer_cols = window // row_count
    chunks = max(1, min(CHUNKS, size_cols // 128))
    width = size_cols // chunks
    row_shift = offsets[led_index, 0]
    col_shift = offsets[led_index, 1]
    measured = amplitudes[0]
    shape_cols = (2, block_rows, outer_cols, row_count)
    row_ids = jnp.arange(window, dtype=jnp.int32)[:, None]

    col_ids = (row_index * size_cols + jnp.arange(size_cols, dtype=jnp.int32))[None, :]
    pupil_full = pupil_at(row_ids, col_ids - col_shift, coeffs, centre)
    pupil_full = lax.optimization_barrier(pupil_full)
    pupils = [
        (pupil_full[0][:, c * width:(c + 1) * width], pupil_full[1][:, c * width:(c + 1) * width])
        for c in range(chunks)
    ]
    regions = []
    for chunk in range(chunks):
        part = spectrum[:, :, chunk * width:(chunk + 1) * width]
        regions.append(lax.all_gather(part, "led", axis=1, tiled=True))
    spreads = []
    for chunk in range(chunks):
        region = regions[chunk]
        if spreads:
            region, _ = lax.optimization_barrier((region, stacked))
        band = lax.dynamic_slice_in_dim(region, row_shift, window, 1)
        pupil_re, pupil_im = pupils[chunk]
        lit_re = pupil_re * band[0] - pupil_im * band[1]
        lit_im = pupil_re * band[1] + pupil_im * band[0]
        half_re, half_im = row_transform(lit_re, lit_im, 1.0)
        stacked = jnp.stack([half_re, half_im])
        spread = lax.all_to_all(stacked, "row", split_axis=1, concat_axis=2, tiled=True)
        spreads.append(spread.reshape(2, block_rows, row_count, width))
    spread_all = jnp.stack(spreads, axis=3).reshape(2, block_rows, row_count * size_cols)
    window_part = lax.dynamic_slice_in_dim(spread_all, col_shift, window, 2)
    field = transform(
        window_part.reshape(shape_cols), "ytr", "ykr", "yjk", outer_cols, row_count, 1.0
    )
    field = field.reshape(2, block_rows, window)
    diff_re, diff_im = correct(field[0], field[1], measured)
    back = transform(
        jnp.stack([diff_re, diff_im]).reshape(shape_cols),
        "ytr",
        "ykr",
        "yjk",
        outer_cols,
        row_count,
        -1.0,
    )
    padded = jnp.zeros((2, block_rows, row_count * size_cols), jnp.float32)
    padded = lax.dynamic_update_slice_in_dim(
        padded, back.reshape(2, block_rows, window), col_shift, 2
    )
    padded = padded.reshape(2, block_rows, row_count, chunks, width)
    gathered_all = []
    for chunk in range(chunks):
        piece = padded[:, :, :, chunk, :].reshape(2, block_rows, row_count * width)
        gathered_all.append(lax.all_to_all(piece, "row", split_axis=2, concat_axis=1, tiled=True))
    results = []
    for chunk in range(chunks):
        gathered = gathered_all[chunk]
        if results:
            gathered, _ = lax.optimization_barrier((gathered, embedded))
        spec_re, spec_im = row_transform(gathered[0], gathered[1], -1.0)
        pupil_re, pupil_im = pupils[chunk]
        upd_re = pupil_re * spec_re + pupil_im * spec_im
        upd_im = pupil_re * spec_im - pupil_im * spec_re
        embedded = jnp.zeros((2, size_rows * led_count, width), jnp.float32)
        embedded = lax.dynamic_update_slice_in_dim(
            embedded, jnp.stack([upd_re, upd_im]), row_shift, 1
        )
        results.append(lax.psum_scatter(embedded, "led", scatter_dimension=1, tiled=True))
    summed = jnp.concatenate(results, axis=2)
    return spectrum + summed


def solution(mesh):
    return jax.shard_map(
        on_device,
        mesh=mesh,
        in_specs=(P(None, "led", "row"), P("led", "row", None), P(), P()),
        out_specs=P(None, "led", "row"),
        check_vma=False,
    )
```

```python
import math

import jax
import jax.numpy as jnp
from jax import lax
from jax.sharding import PartitionSpec as P


SOFTENING = 0.1
HIGHEST_PRECISION = lax.Precision.HIGHEST
CHUNKS = 4


def pupil_at(down_index, across_index, coeffs, centre):
    offset_down = down_index - centre
    offset_across = across_index - centre
    inside = offset_down * offset_down + offset_across * offset_across < centre * centre
    upper_norm = offset_down.astype(jnp.float32) * (1.0 / centre)
    lateral = offset_across.astype(jnp.float32) * (1.0 / centre)
    radial = upper_norm * upper_norm + lateral * lateral
    phases = (
        coeffs[0] * (2.0 * radial - 1.0)
        + coeffs[1] * (upper_norm * upper_norm - lateral * lateral)
        + coeffs[2] * (2.0 * upper_norm * lateral)
        + (3.0 * radial - 2.0) * (coeffs[3] * upper_norm + coeffs[4] * lateral)
        + coeffs[5] * (6.0 * radial * radial - 6.0 * radial + 1.0)
    )
    weight = jnp.where(inside, 1.0, 0.0).astype(jnp.float32)
    return (weight * jnp.cos(phases), weight * jnp.sin(phases))


def tables(outer_size, inner_size, direction):
    length = outer_size * inner_size
    angle_step = direction * 2.0 * math.pi / length
    first_index = jnp.arange(outer_size, dtype=jnp.int32)
    grid_first = first_index[:, None] * first_index[None, :] * inner_size % length
    angles_first = grid_first.astype(jnp.float32) * angle_step
    index_k = jnp.arange(outer_size, dtype=jnp.int32)[:, None, None]
    index_r = jnp.arange(inner_size, dtype=jnp.int32)[None, :, None]
    index_j = jnp.arange(inner_size, dtype=jnp.int32)[None, None, :]
    grid_second = index_r * (index_k + outer_size * index_j) % length
    angles_second = grid_second.astype(jnp.float32) * angle_step
    return (
        jnp.cos(angles_first),
        jnp.sin(angles_first),
        jnp.cos(angles_second),
        jnp.sin(angles_second),
    )


def transform(paired, inputs, middle, output, outer_size, inner_size, direction):
    first_re, first_im, second_re, second_im = tables(outer_size, inner_size, direction)
    scaling = 1.0 / math.sqrt(outer_size * inner_size)
    first_table = jnp.stack([jnp.stack([first_re, first_im]), jnp.stack([-first_im, first_re])])
    second_table = (
        jnp.stack([jnp.stack([second_re, second_im]), jnp.stack([-second_im, second_re])]) * scaling
    )
    middle_pair = jnp.einsum(
        "p" + inputs + ",pqtk->q" + middle, paired, first_table, precision=HIGHEST_PRECISION
    )
    return jnp.einsum(
        "p" + middle + ",pqkrj->q" + output, middle_pair, second_table, precision=HIGHEST_PRECISION
    )


def unit_times(value_re, value_im, turn):
    eighths = round(turn * 8) % 8
    if eighths == 0:
        return value_re, value_im
    if eighths == 2:
        return -value_im, value_re
    if eighths == 4:
        return -value_re, -value_im
    if eighths == 6:
        return value_im, -value_re
    c = math.cos(2.0 * math.pi * turn)
    s = math.sin(2.0 * math.pi * turn)
    return value_re * c - value_im * s, value_re * s + value_im * c


def row_transform(pair_re, pair_im, direction, inner=4):
    length, width = pair_re.shape
    outer = length // inner
    angle_step = direction * 2.0 * math.pi / outer
    index = jnp.arange(outer, dtype=jnp.int32)
    grid = (index[:, None] * index[None, :]) % outer
    angles = grid.astype(jnp.float32) * angle_step
    cos_t = jnp.cos(angles)
    sin_t = jnp.sin(angles)
    table = jnp.concatenate(
        [jnp.concatenate([cos_t, -sin_t], axis=1), jnp.concatenate([sin_t, cos_t], axis=1)], axis=0
    )
    stacked = jnp.concatenate(
        [pair_re.reshape(outer, inner * width), pair_im.reshape(outer, inner * width)], axis=0
    )
    middle = jnp.dot(table, stacked, precision=HIGHEST_PRECISION)
    mid_re = middle[:outer]
    mid_im = middle[outer:]
    scaling = 1.0 / math.sqrt(length)
    twiddled = []
    for r in range(inner):
        part_re = mid_re[:, r * width:(r + 1) * width]
        part_im = mid_im[:, r * width:(r + 1) * width]
        if r == 0:
            twiddled.append((part_re * scaling, part_im * scaling))
            continue
        tw_angle = (r * index % length).astype(jnp.float32) * (direction * 2.0 * math.pi / length)
        tw_re = (jnp.cos(tw_angle) * scaling)[:, None]
        tw_im = (jnp.sin(tw_angle) * scaling)[:, None]
        twiddled.append((part_re * tw_re - part_im * tw_im, part_re * tw_im + part_im * tw_re))
    out_re = []
    out_im = []
    for j in range(inner):
        acc_re = None
        acc_im = None
        for r in range(inner):
            t_re, t_im = unit_times(twiddled[r][0], twiddled[r][1], direction * r * j / inner)
            acc_re = t_re if acc_re is None else acc_re + t_re
            acc_im = t_im if acc_im is None else acc_im + t_im
        out_re.append(acc_re)
        out_im.append(acc_im)
    return jnp.concatenate(out_re, axis=0), jnp.concatenate(out_im, axis=0)


def correct(field_re, field_im, measured):
    magnitude = jnp.sqrt(field_re * field_re + field_im * field_im + SOFTENING)
    factor = measured / magnitude
    return (field_re * factor - field_re, field_im * factor - field_im)


def on_device(spectrum, amplitudes, offsets, coeffs):
    led_count = lax.axis_size("led")
    row_count = lax.axis_size("row")
    led_index = lax.axis_index("led")
    row_index = lax.axis_index("row")
    size_rows = spectrum.shape[1]
    size_cols = spectrum.shape[2]
    window = amplitudes.shape[2]
    centre = window // 2
    block_rows = window // row_count
    outer_cols = window // row_count
    chunks = max(1, min(CHUNKS, size_cols // 128))
    width = size_cols // chunks
    row_shift = offsets[led_index, 0]
    col_shift = offsets[led_index, 1]
    measured = amplitudes[0]
    row_ids = jnp.arange(window, dtype=jnp.int32)[:, None]

    col_ids = (row_index * size_cols + jnp.arange(size_cols, dtype=jnp.int32))[None, :]
    pupil_full = pupil_at(row_ids, col_ids - col_shift, coeffs, centre)
    pupil_full = lax.optimization_barrier(pupil_full)
    pupils = [
        (pupil_full[0][:, c * width:(c + 1) * width], pupil_full[1][:, c * width:(c + 1) * width])
        for c in range(chunks)
    ]
    regions = []
    for chunk in range(chunks):
        part = spectrum[:, :, chunk * width:(chunk + 1) * width]
        regions.append(lax.all_gather(part, "led", axis=1, tiled=True))
    spreads = []
    for chunk in range(chunks):
        region = regions[chunk]
        if spreads:
            region, _ = lax.optimization_barrier((region, stacked))
        band = lax.dynamic_slice_in_dim(region, row_shift, window, 1)
        pupil_re, pupil_im = pupils[chunk]
        lit_re = pupil_re * band[0] - pupil_im * band[1]
        lit_im = pupil_re * band[1] + pupil_im * band[0]
        half_re, half_im = row_transform(lit_re, lit_im, 1.0)
        stacked = jnp.stack([half_re, half_im])
        spread = lax.all_to_all(stacked, "row", split_axis=1, concat_axis=2, tiled=True)
        spreads.append(spread.reshape(2, block_rows, row_count, width))
    spread_all = jnp.stack(spreads, axis=3).reshape(2, block_rows, row_count * size_cols)
    halves = 2 if block_rows % 16 == 0 else 1
    half_rows = block_rows // halves
    shape_half = (2, half_rows, outer_cols, row_count)
    returned = []
    previous = None
    for half in range(halves):
        rows_part = spread_all[:, half * half_rows:(half + 1) * half_rows]
        if previous is not None:
            rows_part, _ = lax.optimization_barrier((rows_part, previous))
        window_part = lax.dynamic_slice_in_dim(rows_part, col_shift, window, 2)
        field = transform(
            window_part.reshape(shape_half), "ytr", "ykr", "yjk", outer_cols, row_count, 1.0
        )
        field = field.reshape(2, half_rows, window)
        diff_re, diff_im = correct(
            field[0], field[1], measured[half * half_rows:(half + 1) * half_rows]
        )
        back = transform(
            jnp.stack([diff_re, diff_im]).reshape(shape_half),
            "ytr",
            "ykr",
            "yjk",
            outer_cols,
            row_count,
            -1.0,
        )
        padded = jnp.zeros((2, half_rows, row_count * size_cols), jnp.float32)
        padded = lax.dynamic_update_slice_in_dim(
            padded, back.reshape(2, half_rows, window), col_shift, 2
        )
        previous = padded
        padded = padded.reshape(2, half_rows, row_count, chunks, width)
        pieces = []
        for chunk in range(chunks):
            piece = padded[:, :, :, chunk, :].reshape(2, half_rows, row_count * width)
            got = lax.all_to_all(piece, "row", split_axis=2, concat_axis=1, tiled=True)
            pieces.append(got.reshape(2, row_count, half_rows, width))
        returned.append(pieces)
    gathered_all = [
        jnp.stack([returned[h][c] for h in range(halves)], axis=2).reshape(2, window, width)
        for c in range(chunks)
    ]
    results = []
    for chunk in range(chunks):
        gathered = gathered_all[chunk]
        if results:
            gathered, _ = lax.optimization_barrier((gathered, embedded))
        spec_re, spec_im = row_transform(gathered[0], gathered[1], -1.0)
        pupil_re, pupil_im = pupils[chunk]
        upd_re = pupil_re * spec_re + pupil_im * spec_im
        upd_im = pupil_re * spec_im - pupil_im * spec_re
        embedded = jnp.zeros((2, size_rows * led_count, width), jnp.float32)
        embedded = lax.dynamic_update_slice_in_dim(
            embedded, jnp.stack([upd_re, upd_im]), row_shift, 1
        )
        results.append(lax.psum_scatter(embedded, "led", scatter_dimension=1, tiled=True))
    summed = jnp.concatenate(results, axis=2)
    return spectrum + summed


def solution(mesh):
    return jax.shard_map(
        on_device,
        mesh=mesh,
        in_specs=(P(None, "led", "row"), P("led", "row", None), P(), P()),
        out_specs=P(None, "led", "row"),
        check_vma=False,
    )
```

```python
import math

import jax
import jax.numpy as jnp
from jax import lax
from jax.sharding import PartitionSpec as P


SOFTENING = 0.1
HIGHEST_PRECISION = lax.Precision.HIGHEST
CHUNKS = 4


def pupil_at(down_index, across_index, coeffs, centre):
    offset_down = down_index - centre
    offset_across = across_index - centre
    inside = offset_down * offset_down + offset_across * offset_across < centre * centre
    upper_norm = offset_down.astype(jnp.float32) * (1.0 / centre)
    lateral = offset_across.astype(jnp.float32) * (1.0 / centre)
    radial = upper_norm * upper_norm + lateral * lateral
    phases = (
        coeffs[0] * (2.0 * radial - 1.0)
        + coeffs[1] * (upper_norm * upper_norm - lateral * lateral)
        + coeffs[2] * (2.0 * upper_norm * lateral)
        + (3.0 * radial - 2.0) * (coeffs[3] * upper_norm + coeffs[4] * lateral)
        + coeffs[5] * (6.0 * radial * radial - 6.0 * radial + 1.0)
    )
    weight = jnp.where(inside, 1.0, 0.0).astype(jnp.float32)
    return (weight * jnp.cos(phases), weight * jnp.sin(phases))


def unit_times(value_re, value_im, turn):
    eighths = round(turn * 8) % 8
    if eighths == 0:
        return value_re, value_im
    if eighths == 2:
        return -value_im, value_re
    if eighths == 4:
        return -value_re, -value_im
    if eighths == 6:
        return value_im, -value_re
    c = math.cos(2.0 * math.pi * turn)
    s = math.sin(2.0 * math.pi * turn)
    return value_re * c - value_im * s, value_re * s + value_im * c


def row_transform(pair_re, pair_im, direction, inner=4):
    length, width = pair_re.shape
    outer = length // inner
    angle_step = direction * 2.0 * math.pi / outer
    index = jnp.arange(outer, dtype=jnp.int32)
    grid = (index[:, None] * index[None, :]) % outer
    angles = grid.astype(jnp.float32) * angle_step
    cos_t = jnp.cos(angles)
    sin_t = jnp.sin(angles)
    table = jnp.concatenate(
        [jnp.concatenate([cos_t, -sin_t], axis=1), jnp.concatenate([sin_t, cos_t], axis=1)], axis=0
    )
    stacked = jnp.concatenate(
        [pair_re.reshape(outer, inner * width), pair_im.reshape(outer, inner * width)], axis=0
    )
    middle = jnp.dot(table, stacked, precision=HIGHEST_PRECISION)
    mid_re = middle[:outer]
    mid_im = middle[outer:]
    scaling = 1.0 / math.sqrt(length)
    twiddled = []
    for r in range(inner):
        part_re = mid_re[:, r * width:(r + 1) * width]
        part_im = mid_im[:, r * width:(r + 1) * width]
        if r == 0:
            twiddled.append((part_re * scaling, part_im * scaling))
            continue
        tw_angle = (r * index % length).astype(jnp.float32) * (direction * 2.0 * math.pi / length)
        tw_re = (jnp.cos(tw_angle) * scaling)[:, None]
        tw_im = (jnp.sin(tw_angle) * scaling)[:, None]
        twiddled.append((part_re * tw_re - part_im * tw_im, part_re * tw_im + part_im * tw_re))
    out_re = []
    out_im = []
    for j in range(inner):
        acc_re = None
        acc_im = None
        for r in range(inner):
            t_re, t_im = unit_times(twiddled[r][0], twiddled[r][1], direction * r * j / inner)
            acc_re = t_re if acc_re is None else acc_re + t_re
            acc_im = t_im if acc_im is None else acc_im + t_im
        out_re.append(acc_re)
        out_im.append(acc_im)
    return jnp.concatenate(out_re, axis=0), jnp.concatenate(out_im, axis=0)


def col_forward(x_re, x_im, direction, inner=8):
    rows, length = x_re.shape
    outer = length // inner
    scaling = 1.0 / math.sqrt(length)
    parts = [(x_re[:, r * outer:(r + 1) * outer], x_im[:, r * outer:(r + 1) * outer]) for r in range(inner)]
    t_index = jnp.arange(outer, dtype=jnp.int32)
    z_re = []
    z_im = []
    for j in range(inner):
        acc_re = None
        acc_im = None
        for r in range(inner):
            t_re, t_im = unit_times(parts[r][0], parts[r][1], direction * r * j / inner)
            acc_re = t_re if acc_re is None else acc_re + t_re
            acc_im = t_im if acc_im is None else acc_im + t_im
        angle = (j * t_index % length).astype(jnp.float32) * (direction * 2.0 * math.pi / length)
        tw_re = (jnp.cos(angle) * scaling)[None, :]
        tw_im = (jnp.sin(angle) * scaling)[None, :]
        z_re.append(acc_re * tw_re - acc_im * tw_im)
        z_im.append(acc_re * tw_im + acc_im * tw_re)
    stacked = jnp.concatenate(
        [jnp.stack(z_re, axis=1).reshape(rows * inner, outer), jnp.stack(z_im, axis=1).reshape(rows * inner, outer)],
        axis=1,
    )
    grid = (t_index[:, None] * t_index[None, :]) % outer
    angles = grid.astype(jnp.float32) * (direction * 2.0 * math.pi / outer)
    cos_t = jnp.cos(angles)
    sin_t = jnp.sin(angles)
    table = jnp.concatenate(
        [jnp.concatenate([cos_t, sin_t], axis=1), jnp.concatenate([-sin_t, cos_t], axis=1)], axis=0
    )
    out = jnp.dot(stacked, table, precision=HIGHEST_PRECISION)
    return out[:, :outer].reshape(rows, inner, outer), out[:, outer:].reshape(rows, inner, outer)


def col_inverse(x_re, x_im, direction):
    rows, inner, outer = x_re.shape
    length = inner * outer
    scaling = 1.0 / math.sqrt(length)
    t_index = jnp.arange(outer, dtype=jnp.int32)
    grid = (t_index[:, None] * t_index[None, :]) % outer
    angles = grid.astype(jnp.float32) * (direction * 2.0 * math.pi / outer)
    cos_t = jnp.cos(angles)
    sin_t = jnp.sin(angles)
    table = jnp.concatenate(
        [jnp.concatenate([cos_t, sin_t], axis=1), jnp.concatenate([-sin_t, cos_t], axis=1)], axis=0
    )
    stacked = jnp.concatenate(
        [x_re.reshape(rows * inner, outer), x_im.reshape(rows * inner, outer)], axis=1
    )
    mid = jnp.dot(stacked, table, precision=HIGHEST_PRECISION)
    mid_re = mid[:, :outer].reshape(rows, inner, outer)
    mid_im = mid[:, outer:].reshape(rows, inner, outer)
    twiddled = []
    for j in range(inner):
        angle = (j * t_index % length).astype(jnp.float32) * (direction * 2.0 * math.pi / length)
        tw_re = (jnp.cos(angle) * scaling)[None, :]
        tw_im = (jnp.sin(angle) * scaling)[None, :]
        m_re = mid_re[:, j]
        m_im = mid_im[:, j]
        twiddled.append((m_re * tw_re - m_im * tw_im, m_re * tw_im + m_im * tw_re))
    out_re = []
    out_im = []
    for r in range(inner):
        acc_re = None
        acc_im = None
        for j in range(inner):
            t_re, t_im = unit_times(twiddled[j][0], twiddled[j][1], direction * r * j / inner)
            acc_re = t_re if acc_re is None else acc_re + t_re
            acc_im = t_im if acc_im is None else acc_im + t_im
        out_re.append(acc_re)
        out_im.append(acc_im)
    return jnp.concatenate(out_re, axis=1), jnp.concatenate(out_im, axis=1)


def correct(field_re, field_im, measured):
    magnitude = jnp.sqrt(field_re * field_re + field_im * field_im + SOFTENING)
    factor = measured / magnitude
    return (field_re * factor - field_re, field_im * factor - field_im)


def on_device(spectrum, amplitudes, offsets, coeffs):
    led_count = lax.axis_size("led")
    row_count = lax.axis_size("row")
    led_index = lax.axis_index("led")
    row_index = lax.axis_index("row")
    size_rows = spectrum.shape[1]
    size_cols = spectrum.shape[2]
    window = amplitudes.shape[2]
    centre = window // 2
    block_rows = window // row_count
    chunks = max(1, min(CHUNKS, size_cols // 128))
    width = size_cols // chunks
    row_shift = offsets[led_index, 0]
    col_shift = offsets[led_index, 1]
    measured = amplitudes[0]
    row_ids = jnp.arange(window, dtype=jnp.int32)[:, None]

    col_ids = (row_index * size_cols + jnp.arange(size_cols, dtype=jnp.int32))[None, :]
    pupil_full = pupil_at(row_ids, col_ids - col_shift, coeffs, centre)
    pupil_full = lax.optimization_barrier(pupil_full)
    pupils = [
        (pupil_full[0][:, c * width:(c + 1) * width], pupil_full[1][:, c * width:(c + 1) * width])
        for c in range(chunks)
    ]
    regions = []
    for chunk in range(chunks):
        part = spectrum[:, :, chunk * width:(chunk + 1) * width]
        regions.append(lax.all_gather(part, "led", axis=1, tiled=True))
    spreads = []
    for chunk in range(chunks):
        region = regions[chunk]
        if spreads:
            region, _ = lax.optimization_barrier((region, stacked))
        band = lax.dynamic_slice_in_dim(region, row_shift, window, 1)
        pupil_re, pupil_im = pupils[chunk]
        lit_re = pupil_re * band[0] - pupil_im * band[1]
        lit_im = pupil_re * band[1] + pupil_im * band[0]
        half_re, half_im = row_transform(lit_re, lit_im, 1.0)
        stacked = jnp.stack([half_re, half_im])
        spread = lax.all_to_all(stacked, "row", split_axis=1, concat_axis=2, tiled=True)
        spreads.append(spread.reshape(2, block_rows, row_count, width))
    spread_all = jnp.stack(spreads, axis=3).reshape(2, block_rows, row_count * size_cols)
    window_part = lax.dynamic_slice_in_dim(spread_all, col_shift, window, 2)
    field_re, field_im = col_forward(window_part[0], window_part[1], 1.0)
    inner_cols = field_re.shape[1]
    measured_perm = measured.reshape(block_rows, window // inner_cols, inner_cols).transpose(0, 2, 1)
    diff_re, diff_im = correct(field_re, field_im, measured_perm)
    back_re, back_im = col_inverse(diff_re, diff_im, -1.0)
    back = jnp.stack([back_re, back_im])
    padded = jnp.zeros((2, block_rows, row_count * size_cols), jnp.float32)
    padded = lax.dynamic_update_slice_in_dim(
        padded, back.reshape(2, block_rows, window), col_shift, 2
    )
    padded = padded.reshape(2, block_rows, row_count, chunks, width)
    gathered_all = []
    for chunk in range(chunks):
        piece = padded[:, :, :, chunk, :].reshape(2, block_rows, row_count * width)
        gathered_all.append(lax.all_to_all(piece, "row", split_axis=2, concat_axis=1, tiled=True))
    results = []
    for chunk in range(chunks):
        gathered = gathered_all[chunk]
        if results:
            gathered, _ = lax.optimization_barrier((gathered, embedded))
        spec_re, spec_im = row_transform(gathered[0], gathered[1], -1.0)
        pupil_re, pupil_im = pupils[chunk]
        upd_re = pupil_re * spec_re + pupil_im * spec_im
        upd_im = pupil_re * spec_im - pupil_im * spec_re
        embedded = jnp.zeros((2, size_rows * led_count, width), jnp.float32)
        embedded = lax.dynamic_update_slice_in_dim(
            embedded, jnp.stack([upd_re, upd_im]), row_shift, 1
        )
        results.append(lax.psum_scatter(embedded, "led", scatter_dimension=1, tiled=True))
    summed = jnp.concatenate(results, axis=2)
    return spectrum + summed


def solution(mesh):
    return jax.shard_map(
        on_device,
        mesh=mesh,
        in_specs=(P(None, "led", "row"), P("led", "row", None), P(), P()),
        out_specs=P(None, "led", "row"),
        check_vma=False,
    )
```

```python
import math

import jax
import jax.numpy as jnp
from jax import lax
from jax.sharding import PartitionSpec as P


SOFTENING = 0.1
HIGHEST_PRECISION = lax.Precision.HIGHEST
CHUNKS = 4


def pupil_at(down_index, across_index, coeffs, centre):
    offset_down = down_index - centre
    offset_across = across_index - centre
    inside = offset_down * offset_down + offset_across * offset_across < centre * centre
    upper_norm = offset_down.astype(jnp.float32) * (1.0 / centre)
    lateral = offset_across.astype(jnp.float32) * (1.0 / centre)
    radial = upper_norm * upper_norm + lateral * lateral
    phases = (
        coeffs[0] * (2.0 * radial - 1.0)
        + coeffs[1] * (upper_norm * upper_norm - lateral * lateral)
        + coeffs[2] * (2.0 * upper_norm * lateral)
        + (3.0 * radial - 2.0) * (coeffs[3] * upper_norm + coeffs[4] * lateral)
        + coeffs[5] * (6.0 * radial * radial - 6.0 * radial + 1.0)
    )
    weight = jnp.where(inside, 1.0, 0.0).astype(jnp.float32)
    return (weight * jnp.cos(phases), weight * jnp.sin(phases))


def tables(outer_size, inner_size, direction):
    length = outer_size * inner_size
    angle_step = direction * 2.0 * math.pi / length
    first_index = jnp.arange(outer_size, dtype=jnp.int32)
    grid_first = first_index[:, None] * first_index[None, :] * inner_size % length
    angles_first = grid_first.astype(jnp.float32) * angle_step
    index_k = jnp.arange(outer_size, dtype=jnp.int32)[:, None, None]
    index_r = jnp.arange(inner_size, dtype=jnp.int32)[None, :, None]
    index_j = jnp.arange(inner_size, dtype=jnp.int32)[None, None, :]
    grid_second = index_r * (index_k + outer_size * index_j) % length
    angles_second = grid_second.astype(jnp.float32) * angle_step
    return (
        jnp.cos(angles_first),
        jnp.sin(angles_first),
        jnp.cos(angles_second),
        jnp.sin(angles_second),
    )


def transform(paired, inputs, middle, output, outer_size, inner_size, direction):
    first_re, first_im, second_re, second_im = tables(outer_size, inner_size, direction)
    scaling = 1.0 / math.sqrt(outer_size * inner_size)
    first_table = jnp.stack([jnp.stack([first_re, first_im]), jnp.stack([-first_im, first_re])])
    second_table = (
        jnp.stack([jnp.stack([second_re, second_im]), jnp.stack([-second_im, second_re])]) * scaling
    )
    middle_pair = jnp.einsum(
        "p" + inputs + ",pqtk->q" + middle, paired, first_table, precision=HIGHEST_PRECISION
    )
    return jnp.einsum(
        "p" + middle + ",pqkrj->q" + output, middle_pair, second_table, precision=HIGHEST_PRECISION
    )


def unit_times(value_re, value_im, turn):
    eighths = round(turn * 8) % 8
    if eighths == 0:
        return value_re, value_im
    if eighths == 2:
        return -value_im, value_re
    if eighths == 4:
        return -value_re, -value_im
    if eighths == 6:
        return value_im, -value_re
    c = math.cos(2.0 * math.pi * turn)
    s = math.sin(2.0 * math.pi * turn)
    return value_re * c - value_im * s, value_re * s + value_im * c


def row_transform(pair_re, pair_im, direction, inner=4):
    length, width = pair_re.shape
    outer = length // inner
    angle_step = direction * 2.0 * math.pi / outer
    index = jnp.arange(outer, dtype=jnp.int32)
    grid = (index[:, None] * index[None, :]) % outer
    angles = grid.astype(jnp.float32) * angle_step
    cos_t = jnp.cos(angles)
    sin_t = jnp.sin(angles)
    table = jnp.concatenate(
        [jnp.concatenate([cos_t, -sin_t], axis=1), jnp.concatenate([sin_t, cos_t], axis=1)], axis=0
    )
    stacked = jnp.concatenate(
        [pair_re.reshape(outer, inner * width), pair_im.reshape(outer, inner * width)], axis=0
    )
    middle = jnp.dot(table, stacked, precision=HIGHEST_PRECISION)
    mid_re = middle[:outer]
    mid_im = middle[outer:]
    scaling = 1.0 / math.sqrt(length)
    twiddled = []
    for r in range(inner):
        part_re = mid_re[:, r * width:(r + 1) * width]
        part_im = mid_im[:, r * width:(r + 1) * width]
        if r == 0:
            twiddled.append((part_re * scaling, part_im * scaling))
            continue
        tw_angle = (r * index % length).astype(jnp.float32) * (direction * 2.0 * math.pi / length)
        tw_re = (jnp.cos(tw_angle) * scaling)[:, None]
        tw_im = (jnp.sin(tw_angle) * scaling)[:, None]
        twiddled.append((part_re * tw_re - part_im * tw_im, part_re * tw_im + part_im * tw_re))
    out_re = []
    out_im = []
    for j in range(inner):
        acc_re = None
        acc_im = None
        for r in range(inner):
            t_re, t_im = unit_times(twiddled[r][0], twiddled[r][1], direction * r * j / inner)
            acc_re = t_re if acc_re is None else acc_re + t_re
            acc_im = t_im if acc_im is None else acc_im + t_im
        out_re.append(acc_re)
        out_im.append(acc_im)
    return jnp.concatenate(out_re, axis=0), jnp.concatenate(out_im, axis=0)


def correct(field_re, field_im, measured):
    magnitude = jnp.sqrt(field_re * field_re + field_im * field_im + SOFTENING)
    factor = measured / magnitude
    return (field_re * factor - field_re, field_im * factor - field_im)


def on_device(spectrum, amplitudes, offsets, coeffs):
    led_count = lax.axis_size("led")
    row_count = lax.axis_size("row")
    led_index = lax.axis_index("led")
    row_index = lax.axis_index("row")
    size_rows = spectrum.shape[1]
    size_cols = spectrum.shape[2]
    window = amplitudes.shape[2]
    centre = window // 2
    block_rows = window // row_count
    outer_cols = window // row_count
    chunks = max(1, min(CHUNKS, size_cols // 128))
    width = size_cols // chunks
    row_shift = offsets[led_index, 0]
    col_shift = offsets[led_index, 1]
    measured = amplitudes[0]
    shape_cols = (2, block_rows, outer_cols, row_count)
    row_ids = jnp.arange(window, dtype=jnp.int32)[:, None]

    col_ids = (row_index * size_cols + jnp.arange(size_cols, dtype=jnp.int32))[None, :]
    pupil_full = pupil_at(row_ids, col_ids - col_shift, coeffs, centre)
    pupil_full = lax.optimization_barrier(pupil_full)
    pupils = [
        (pupil_full[0][:, c * width:(c + 1) * width], pupil_full[1][:, c * width:(c + 1) * width])
        for c in range(chunks)
    ]
    regions = []
    for chunk in range(chunks):
        part = spectrum[:, :, chunk * width:(chunk + 1) * width]
        regions.append(lax.all_gather(part, "led", axis=1, tiled=True))
    spreads = []
    for chunk in range(chunks):
        region = regions[chunk]
        if spreads:
            region, _ = lax.optimization_barrier((region, stacked))
        band = lax.dynamic_slice_in_dim(region, row_shift, window, 1)
        pupil_re, pupil_im = pupils[chunk]
        lit_re = pupil_re * band[0] - pupil_im * band[1]
        lit_im = pupil_re * band[1] + pupil_im * band[0]
        half_re, half_im = row_transform(lit_re, lit_im, 1.0)
        stacked = jnp.stack([half_re, half_im])
        spread = lax.all_to_all(stacked, "row", split_axis=1, concat_axis=2, tiled=True)
        spreads.append(spread.reshape(2, block_rows, row_count, width))
    folds = row_count * size_cols // window
    per_fold = row_count // folds
    folded = []
    for spread in spreads:
        total = spread[:, :, :per_fold]
        for f in range(1, folds):
            total = total + spread[:, :, f * per_fold:(f + 1) * per_fold]
        folded.append(total)
    window_part = jnp.stack(folded, axis=3).reshape(2, block_rows, window)
    field = transform(
        window_part.reshape(shape_cols), "ytr", "ykr", "yjk", outer_cols, row_count, 1.0
    )
    field = field.reshape(2, block_rows, window)
    diff_re, diff_im = correct(field[0], field[1], measured)
    back = transform(
        jnp.stack([diff_re, diff_im]).reshape(shape_cols),
        "ytr",
        "ykr",
        "yjk",
        outer_cols,
        row_count,
        -1.0,
    )
    back = back.reshape(2, block_rows, per_fold, chunks, width)
    gathered_all = []
    for chunk in range(chunks):
        piece = jnp.concatenate([back[:, :, :, chunk, :]] * folds, axis=2)
        piece = piece.reshape(2, block_rows, row_count * width)
        gathered_all.append(lax.all_to_all(piece, "row", split_axis=2, concat_axis=1, tiled=True))
    results = []
    for chunk in range(chunks):
        gathered = gathered_all[chunk]
        if results:
            gathered, _ = lax.optimization_barrier((gathered, embedded))
        spec_re, spec_im = row_transform(gathered[0], gathered[1], -1.0)
        pupil_re, pupil_im = pupils[chunk]
        upd_re = pupil_re * spec_re + pupil_im * spec_im
        upd_im = pupil_re * spec_im - pupil_im * spec_re
        embedded = jnp.zeros((2, size_rows * led_count, width), jnp.float32)
        embedded = lax.dynamic_update_slice_in_dim(
            embedded, jnp.stack([upd_re, upd_im]), row_shift, 1
        )
        results.append(lax.psum_scatter(embedded, "led", scatter_dimension=1, tiled=True))
    summed = jnp.concatenate(results, axis=2)
    return spectrum + summed


def solution(mesh):
    return jax.shard_map(
        on_device,
        mesh=mesh,
        in_specs=(P(None, "led", "row"), P("led", "row", None), P(), P()),
        out_specs=P(None, "led", "row"),
        check_vma=False,
    )
```

```python
import math

import jax
import jax.numpy as jnp
from jax import lax
from jax.sharding import PartitionSpec as P


SOFTENING = 0.1
HIGHEST_PRECISION = lax.Precision.HIGHEST
CHUNKS = 4


def pupil_at(down_index, across_index, coeffs, centre):
    offset_down = down_index - centre
    offset_across = across_index - centre
    inside = offset_down * offset_down + offset_across * offset_across < centre * centre
    upper_norm = offset_down.astype(jnp.float32) * (1.0 / centre)
    lateral = offset_across.astype(jnp.float32) * (1.0 / centre)
    radial = upper_norm * upper_norm + lateral * lateral
    phases = (
        coeffs[0] * (2.0 * radial - 1.0)
        + coeffs[1] * (upper_norm * upper_norm - lateral * lateral)
        + coeffs[2] * (2.0 * upper_norm * lateral)
        + (3.0 * radial - 2.0) * (coeffs[3] * upper_norm + coeffs[4] * lateral)
        + coeffs[5] * (6.0 * radial * radial - 6.0 * radial + 1.0)
    )
    weight = jnp.where(inside, 1.0, 0.0).astype(jnp.float32)
    return (weight * jnp.cos(phases), weight * jnp.sin(phases))


def tables(outer_size, inner_size, direction):
    length = outer_size * inner_size
    angle_step = direction * 2.0 * math.pi / length
    first_index = jnp.arange(outer_size, dtype=jnp.int32)
    grid_first = first_index[:, None] * first_index[None, :] * inner_size % length
    angles_first = grid_first.astype(jnp.float32) * angle_step
    index_k = jnp.arange(outer_size, dtype=jnp.int32)[:, None, None]
    index_r = jnp.arange(inner_size, dtype=jnp.int32)[None, :, None]
    index_j = jnp.arange(inner_size, dtype=jnp.int32)[None, None, :]
    grid_second = index_r * (index_k + outer_size * index_j) % length
    angles_second = grid_second.astype(jnp.float32) * angle_step
    return (
        jnp.cos(angles_first),
        jnp.sin(angles_first),
        jnp.cos(angles_second),
        jnp.sin(angles_second),
    )


def transform(paired, inputs, middle, output, outer_size, inner_size, direction):
    first_re, first_im, second_re, second_im = tables(outer_size, inner_size, direction)
    scaling = 1.0 / math.sqrt(outer_size * inner_size)
    first_table = jnp.stack([jnp.stack([first_re, first_im]), jnp.stack([-first_im, first_re])])
    second_table = (
        jnp.stack([jnp.stack([second_re, second_im]), jnp.stack([-second_im, second_re])]) * scaling
    )
    middle_pair = jnp.einsum(
        "p" + inputs + ",pqtk->q" + middle, paired, first_table, precision=HIGHEST_PRECISION
    )
    return jnp.einsum(
        "p" + middle + ",pqkrj->q" + output, middle_pair, second_table, precision=HIGHEST_PRECISION
    )


def unit_times(value_re, value_im, turn):
    eighths = round(turn * 8) % 8
    if eighths == 0:
        return value_re, value_im
    if eighths == 2:
        return -value_im, value_re
    if eighths == 4:
        return -value_re, -value_im
    if eighths == 6:
        return value_im, -value_re
    c = math.cos(2.0 * math.pi * turn)
    s = math.sin(2.0 * math.pi * turn)
    return value_re * c - value_im * s, value_re * s + value_im * c


def row_transform(pair_re, pair_im, direction, inner=4):
    length, width = pair_re.shape
    outer = length // inner
    angle_step = direction * 2.0 * math.pi / outer
    index = jnp.arange(outer, dtype=jnp.int32)
    grid = (index[:, None] * index[None, :]) % outer
    angles = grid.astype(jnp.float32) * angle_step
    cos_t = jnp.cos(angles)
    sin_t = jnp.sin(angles)
    table = jnp.concatenate(
        [jnp.concatenate([cos_t, -sin_t], axis=1), jnp.concatenate([sin_t, cos_t], axis=1)], axis=0
    )
    stacked = jnp.concatenate(
        [pair_re.reshape(outer, inner * width), pair_im.reshape(outer, inner * width)], axis=0
    )
    middle = jnp.dot(table, stacked, precision=HIGHEST_PRECISION)
    mid_re = middle[:outer]
    mid_im = middle[outer:]
    scaling = 1.0 / math.sqrt(length)
    twiddled = []
    for r in range(inner):
        part_re = mid_re[:, r * width:(r + 1) * width]
        part_im = mid_im[:, r * width:(r + 1) * width]
        if r == 0:
            twiddled.append((part_re * scaling, part_im * scaling))
            continue
        tw_angle = (r * index % length).astype(jnp.float32) * (direction * 2.0 * math.pi / length)
        tw_re = (jnp.cos(tw_angle) * scaling)[:, None]
        tw_im = (jnp.sin(tw_angle) * scaling)[:, None]
        twiddled.append((part_re * tw_re - part_im * tw_im, part_re * tw_im + part_im * tw_re))
    out_re = []
    out_im = []
    for j in range(inner):
        acc_re = None
        acc_im = None
        for r in range(inner):
            t_re, t_im = unit_times(twiddled[r][0], twiddled[r][1], direction * r * j / inner)
            acc_re = t_re if acc_re is None else acc_re + t_re
            acc_im = t_im if acc_im is None else acc_im + t_im
        out_re.append(acc_re)
        out_im.append(acc_im)
    return jnp.concatenate(out_re, axis=0), jnp.concatenate(out_im, axis=0)


def correct(field_re, field_im, measured):
    magnitude = jnp.sqrt(field_re * field_re + field_im * field_im + SOFTENING)
    factor = measured / magnitude
    return (field_re * factor - field_re, field_im * factor - field_im)


def on_device(spectrum, amplitudes, offsets, coeffs):
    led_count = lax.axis_size("led")
    row_count = lax.axis_size("row")
    led_index = lax.axis_index("led")
    row_index = lax.axis_index("row")
    size_rows = spectrum.shape[1]
    size_cols = spectrum.shape[2]
    window = amplitudes.shape[2]
    centre = window // 2
    block_rows = window // row_count
    outer_cols = window // row_count
    chunks = max(1, min(CHUNKS, size_cols // 128))
    width = size_cols // chunks
    row_shift = offsets[led_index, 0]
    col_shift = offsets[led_index, 1]
    measured = amplitudes[0]
    shape_cols = (2, block_rows, outer_cols, row_count)
    row_ids = jnp.arange(window, dtype=jnp.int32)[:, None]

    col_ids = (row_index * size_cols + jnp.arange(size_cols, dtype=jnp.int32))[None, :]
    pupil_full = pupil_at(row_ids, col_ids - col_shift, coeffs, centre)
    pupil_full = lax.optimization_barrier(pupil_full)
    pupils = [
        (pupil_full[0][:, c * width:(c + 1) * width], pupil_full[1][:, c * width:(c + 1) * width])
        for c in range(chunks)
    ]
    regions = []
    for chunk in range(chunks):
        part = spectrum[:, :, chunk * width:(chunk + 1) * width]
        regions.append(lax.all_gather(part, "led", axis=1, tiled=True))
    spreads = []
    for chunk in range(chunks):
        region = regions[chunk]
        if spreads:
            region, _ = lax.optimization_barrier((region, stacked))
        band = lax.dynamic_slice_in_dim(region, row_shift, window, 1)
        pupil_re, pupil_im = pupils[chunk]
        lit_re = pupil_re * band[0] - pupil_im * band[1]
        lit_im = pupil_re * band[1] + pupil_im * band[0]
        half_re, half_im = row_transform(lit_re, lit_im, 1.0)
        stacked = jnp.stack(
            [
                half_re.reshape(row_count, block_rows, width),
                half_im.reshape(row_count, block_rows, width),
            ],
            axis=1,
        )
        spread = lax.all_to_all(stacked, "row", split_axis=0, concat_axis=0, tiled=True)
        spreads.append(spread)
    folds = row_count * size_cols // window
    per_fold = row_count // folds
    folded = []
    for spread in spreads:
        total = spread[:per_fold]
        for f in range(1, folds):
            total = total + spread[f * per_fold:(f + 1) * per_fold]
        folded.append(total)
    window_part = (
        jnp.stack(folded, axis=1).transpose(2, 3, 0, 1, 4).reshape(2, block_rows, window)
    )
    field = transform(
        window_part.reshape(shape_cols), "ytr", "ykr", "yjk", outer_cols, row_count, 1.0
    )
    field = field.reshape(2, block_rows, window)
    diff_re, diff_im = correct(field[0], field[1], measured)
    back = transform(
        jnp.stack([diff_re, diff_im]).reshape(shape_cols),
        "ytr",
        "ykr",
        "yjk",
        outer_cols,
        row_count,
        -1.0,
    )
    back = back.reshape(2, block_rows, per_fold, chunks, width)
    gathered_all = []
    for chunk in range(chunks):
        piece = back[:, :, :, chunk, :].transpose(2, 0, 1, 3)
        piece = jnp.concatenate([piece] * folds, axis=0)
        gathered_all.append(lax.all_to_all(piece, "row", split_axis=0, concat_axis=0, tiled=True))
    results = []
    for chunk in range(chunks):
        gathered = gathered_all[chunk]
        if results:
            gathered, _ = lax.optimization_barrier((gathered, embedded))
        spec_re, spec_im = row_transform(
            gathered[:, 0].reshape(window, width), gathered[:, 1].reshape(window, width), -1.0
        )
        pupil_re, pupil_im = pupils[chunk]
        upd_re = pupil_re * spec_re + pupil_im * spec_im
        upd_im = pupil_re * spec_im - pupil_im * spec_re
        embedded = jnp.zeros((2, size_rows * led_count, width), jnp.float32)
        embedded = lax.dynamic_update_slice_in_dim(
            embedded, jnp.stack([upd_re, upd_im]), row_shift, 1
        )
        results.append(lax.psum_scatter(embedded, "led", scatter_dimension=1, tiled=True))
    summed = jnp.concatenate(results, axis=2)
    return spectrum + summed


def solution(mesh):
    return jax.shard_map(
        on_device,
        mesh=mesh,
        in_specs=(P(None, "led", "row"), P("led", "row", None), P(), P()),
        out_specs=P(None, "led", "row"),
        check_vma=False,
    )
```

```python
import math

import jax
import jax.numpy as jnp
from jax import lax
from jax.sharding import PartitionSpec as P


SOFTENING = 0.1
HIGHEST_PRECISION = lax.Precision.HIGHEST
CHUNKS = 4


def pupil_at(down_index, across_index, coeffs, centre):
    offset_down = down_index - centre
    offset_across = across_index - centre
    inside = offset_down * offset_down + offset_across * offset_across < centre * centre
    upper_norm = offset_down.astype(jnp.float32) * (1.0 / centre)
    lateral = offset_across.astype(jnp.float32) * (1.0 / centre)
    radial = upper_norm * upper_norm + lateral * lateral
    phases = (
        coeffs[0] * (2.0 * radial - 1.0)
        + coeffs[1] * (upper_norm * upper_norm - lateral * lateral)
        + coeffs[2] * (2.0 * upper_norm * lateral)
        + (3.0 * radial - 2.0) * (coeffs[3] * upper_norm + coeffs[4] * lateral)
        + coeffs[5] * (6.0 * radial * radial - 6.0 * radial + 1.0)
    )
    weight = jnp.where(inside, 1.0, 0.0).astype(jnp.float32)
    return (weight * jnp.cos(phases), weight * jnp.sin(phases))


def tables(outer_size, inner_size, direction):
    length = outer_size * inner_size
    angle_step = direction * 2.0 * math.pi / length
    first_index = jnp.arange(outer_size, dtype=jnp.int32)
    grid_first = first_index[:, None] * first_index[None, :] * inner_size % length
    angles_first = grid_first.astype(jnp.float32) * angle_step
    index_k = jnp.arange(outer_size, dtype=jnp.int32)[:, None, None]
    index_r = jnp.arange(inner_size, dtype=jnp.int32)[None, :, None]
    index_j = jnp.arange(inner_size, dtype=jnp.int32)[None, None, :]
    grid_second = index_r * (index_k + outer_size * index_j) % length
    angles_second = grid_second.astype(jnp.float32) * angle_step
    return (
        jnp.cos(angles_first),
        jnp.sin(angles_first),
        jnp.cos(angles_second),
        jnp.sin(angles_second),
    )


def transform(paired, inputs, middle, output, outer_size, inner_size, direction):
    first_re, first_im, second_re, second_im = tables(outer_size, inner_size, direction)
    scaling = 1.0 / math.sqrt(outer_size * inner_size)
    first_table = jnp.stack([jnp.stack([first_re, first_im]), jnp.stack([-first_im, first_re])])
    second_table = (
        jnp.stack([jnp.stack([second_re, second_im]), jnp.stack([-second_im, second_re])]) * scaling
    )
    middle_pair = jnp.einsum(
        "p" + inputs + ",pqtk->q" + middle, paired, first_table, precision=HIGHEST_PRECISION
    )
    return jnp.einsum(
        "p" + middle + ",pqkrj->q" + output, middle_pair, second_table, precision=lax.Precision.HIGH
    )


def unit_times(value_re, value_im, turn):
    eighths = round(turn * 8) % 8
    if eighths == 0:
        return value_re, value_im
    if eighths == 2:
        return -value_im, value_re
    if eighths == 4:
        return -value_re, -value_im
    if eighths == 6:
        return value_im, -value_re
    c = math.cos(2.0 * math.pi * turn)
    s = math.sin(2.0 * math.pi * turn)
    return value_re * c - value_im * s, value_re * s + value_im * c


def row_transform(pair_re, pair_im, direction, inner=4):
    length, width = pair_re.shape
    outer = length // inner
    angle_step = direction * 2.0 * math.pi / outer
    index = jnp.arange(outer, dtype=jnp.int32)
    grid = (index[:, None] * index[None, :]) % outer
    angles = grid.astype(jnp.float32) * angle_step
    cos_t = jnp.cos(angles)
    sin_t = jnp.sin(angles)
    table = jnp.concatenate(
        [jnp.concatenate([cos_t, -sin_t], axis=1), jnp.concatenate([sin_t, cos_t], axis=1)], axis=0
    )
    stacked = jnp.concatenate(
        [pair_re.reshape(outer, inner * width), pair_im.reshape(outer, inner * width)], axis=0
    )
    middle = jnp.dot(table, stacked, precision=HIGHEST_PRECISION)
    mid_re = middle[:outer]
    mid_im = middle[outer:]
    scaling = 1.0 / math.sqrt(length)
    twiddled = []
    for r in range(inner):
        part_re = mid_re[:, r * width:(r + 1) * width]
        part_im = mid_im[:, r * width:(r + 1) * width]
        if r == 0:
            twiddled.append((part_re * scaling, part_im * scaling))
            continue
        tw_angle = (r * index % length).astype(jnp.float32) * (direction * 2.0 * math.pi / length)
        tw_re = (jnp.cos(tw_angle) * scaling)[:, None]
        tw_im = (jnp.sin(tw_angle) * scaling)[:, None]
        twiddled.append((part_re * tw_re - part_im * tw_im, part_re * tw_im + part_im * tw_re))
    out_re = []
    out_im = []
    for j in range(inner):
        acc_re = None
        acc_im = None
        for r in range(inner):
            t_re, t_im = unit_times(twiddled[r][0], twiddled[r][1], direction * r * j / inner)
            acc_re = t_re if acc_re is None else acc_re + t_re
            acc_im = t_im if acc_im is None else acc_im + t_im
        out_re.append(acc_re)
        out_im.append(acc_im)
    return jnp.concatenate(out_re, axis=0), jnp.concatenate(out_im, axis=0)


def correct(field_re, field_im, measured):
    magnitude = jnp.sqrt(field_re * field_re + field_im * field_im + SOFTENING)
    factor = measured / magnitude
    return (field_re * factor - field_re, field_im * factor - field_im)


def on_device(spectrum, amplitudes, offsets, coeffs):
    led_count = lax.axis_size("led")
    row_count = lax.axis_size("row")
    led_index = lax.axis_index("led")
    row_index = lax.axis_index("row")
    size_rows = spectrum.shape[1]
    size_cols = spectrum.shape[2]
    window = amplitudes.shape[2]
    centre = window // 2
    block_rows = window // row_count
    outer_cols = window // row_count
    chunks = max(1, min(CHUNKS, size_cols // 128))
    width = size_cols // chunks
    row_shift = offsets[led_index, 0]
    col_shift = offsets[led_index, 1]
    measured = amplitudes[0]
    shape_cols = (2, block_rows, outer_cols, row_count)
    row_ids = jnp.arange(window, dtype=jnp.int32)[:, None]

    col_ids = (row_index * size_cols + jnp.arange(size_cols, dtype=jnp.int32))[None, :]
    pupil_full = pupil_at(row_ids, col_ids - col_shift, coeffs, centre)
    pupil_full = lax.optimization_barrier(pupil_full)
    pupils = [
        (pupil_full[0][:, c * width:(c + 1) * width], pupil_full[1][:, c * width:(c + 1) * width])
        for c in range(chunks)
    ]
    regions = []
    for chunk in range(chunks):
        part = spectrum[:, :, chunk * width:(chunk + 1) * width]
        regions.append(lax.all_gather(part, "led", axis=1, tiled=True))
    spreads = []
    for chunk in range(chunks):
        region = regions[chunk]
        if spreads:
            region, _ = lax.optimization_barrier((region, stacked))
        band = lax.dynamic_slice_in_dim(region, row_shift, window, 1)
        pupil_re, pupil_im = pupils[chunk]
        lit_re = pupil_re * band[0] - pupil_im * band[1]
        lit_im = pupil_re * band[1] + pupil_im * band[0]
        half_re, half_im = row_transform(lit_re, lit_im, 1.0)
        stacked = jnp.stack(
            [
                half_re.reshape(row_count, block_rows, width),
                half_im.reshape(row_count, block_rows, width),
            ],
            axis=1,
        )
        spread = lax.all_to_all(stacked, "row", split_axis=0, concat_axis=0, tiled=True)
        spreads.append(spread)
    folds = row_count * size_cols // window
    per_fold = row_count // folds
    folded = []
    for spread in spreads:
        total = spread[:per_fold]
        for f in range(1, folds):
            total = total + spread[f * per_fold:(f + 1) * per_fold]
        folded.append(total)
    window_part = (
        jnp.stack(folded, axis=1).transpose(2, 3, 0, 1, 4).reshape(2, block_rows, window)
    )
    field = transform(
        window_part.reshape(shape_cols), "ytr", "ykr", "yjk", outer_cols, row_count, 1.0
    )
    field = field.reshape(2, block_rows, window)
    diff_re, diff_im = correct(field[0], field[1], measured)
    back = transform(
        jnp.stack([diff_re, diff_im]).reshape(shape_cols),
        "ytr",
        "ykr",
        "yjk",
        outer_cols,
        row_count,
        -1.0,
    )
    back = back.reshape(2, block_rows, per_fold, chunks, width)
    gathered_all = []
    for chunk in range(chunks):
        piece = back[:, :, :, chunk, :].transpose(2, 0, 1, 3)
        piece = jnp.concatenate([piece] * folds, axis=0)
        gathered_all.append(lax.all_to_all(piece, "row", split_axis=0, concat_axis=0, tiled=True))
    results = []
    for chunk in range(chunks):
        gathered = gathered_all[chunk]
        if results:
            gathered, _ = lax.optimization_barrier((gathered, embedded))
        spec_re, spec_im = row_transform(
            gathered[:, 0].reshape(window, width), gathered[:, 1].reshape(window, width), -1.0
        )
        pupil_re, pupil_im = pupils[chunk]
        upd_re = pupil_re * spec_re + pupil_im * spec_im
        upd_im = pupil_re * spec_im - pupil_im * spec_re
        embedded = jnp.zeros((2, size_rows * led_count, width), jnp.float32)
        embedded = lax.dynamic_update_slice_in_dim(
            embedded, jnp.stack([upd_re, upd_im]), row_shift, 1
        )
        results.append(lax.psum_scatter(embedded, "led", scatter_dimension=1, tiled=True))
    out = spectrum
    for chunk in range(chunks):
        added = spectrum[:, :, chunk * width:(chunk + 1) * width] + results[chunk]
        out = lax.dynamic_update_slice_in_dim(out, added, chunk * width, 2)
    return out


def solution(mesh):
    return jax.shard_map(
        on_device,
        mesh=mesh,
        in_specs=(P(None, "led", "row"), P("led", "row", None), P(), P()),
        out_specs=P(None, "led", "row"),
        check_vma=False,
    )
```

```python
import math

import jax
import jax.numpy as jnp
from jax import lax
from jax.sharding import PartitionSpec as P


SOFTENING = 0.1
HIGHEST_PRECISION = lax.Precision.HIGHEST
CHUNKS = 4


def pupil_at(down_index, across_index, coeffs, centre):
    offset_down = down_index - centre
    offset_across = across_index - centre
    inside = offset_down * offset_down + offset_across * offset_across < centre * centre
    upper_norm = offset_down.astype(jnp.float32) * (1.0 / centre)
    lateral = offset_across.astype(jnp.float32) * (1.0 / centre)
    radial = upper_norm * upper_norm + lateral * lateral
    phases = (
        coeffs[0] * (2.0 * radial - 1.0)
        + coeffs[1] * (upper_norm * upper_norm - lateral * lateral)
        + coeffs[2] * (2.0 * upper_norm * lateral)
        + (3.0 * radial - 2.0) * (coeffs[3] * upper_norm + coeffs[4] * lateral)
        + coeffs[5] * (6.0 * radial * radial - 6.0 * radial + 1.0)
    )
    weight = jnp.where(inside, 1.0, 0.0).astype(jnp.float32)
    return (weight * jnp.cos(phases), weight * jnp.sin(phases))


def tables(outer_size, inner_size, direction):
    length = outer_size * inner_size
    angle_step = direction * 2.0 * math.pi / length
    first_index = jnp.arange(outer_size, dtype=jnp.int32)
    grid_first = first_index[:, None] * first_index[None, :] * inner_size % length
    angles_first = grid_first.astype(jnp.float32) * angle_step
    index_k = jnp.arange(outer_size, dtype=jnp.int32)[:, None, None]
    index_r = jnp.arange(inner_size, dtype=jnp.int32)[None, :, None]
    index_j = jnp.arange(inner_size, dtype=jnp.int32)[None, None, :]
    grid_second = index_r * (index_k + outer_size * index_j) % length
    angles_second = grid_second.astype(jnp.float32) * angle_step
    return (
        jnp.cos(angles_first),
        jnp.sin(angles_first),
        jnp.cos(angles_second),
        jnp.sin(angles_second),
    )


def transform(paired, inputs, middle, output, outer_size, inner_size, direction):
    first_re, first_im, second_re, second_im = tables(outer_size, inner_size, direction)
    scaling = 1.0 / math.sqrt(outer_size * inner_size)
    first_table = jnp.stack([jnp.stack([first_re, first_im]), jnp.stack([-first_im, first_re])])
    second_table = (
        jnp.stack([jnp.stack([second_re, second_im]), jnp.stack([-second_im, second_re])]) * scaling
    )
    middle_pair = jnp.einsum(
        "p" + inputs + ",pqtk->q" + middle, paired, first_table, precision=HIGHEST_PRECISION
    )
    return jnp.einsum(
        "p" + middle + ",pqkrj->q" + output, middle_pair, second_table, precision=lax.Precision.HIGH
    )


def unit_times(value_re, value_im, turn):
    eighths = round(turn * 8) % 8
    if eighths == 0:
        return value_re, value_im
    if eighths == 2:
        return -value_im, value_re
    if eighths == 4:
        return -value_re, -value_im
    if eighths == 6:
        return value_im, -value_re
    c = math.cos(2.0 * math.pi * turn)
    s = math.sin(2.0 * math.pi * turn)
    return value_re * c - value_im * s, value_re * s + value_im * c


def row_transform(pair_re, pair_im, direction, inner=4, precision=HIGHEST_PRECISION):
    length, width = pair_re.shape
    outer = length // inner
    angle_step = direction * 2.0 * math.pi / outer
    index = jnp.arange(outer, dtype=jnp.int32)
    grid = (index[:, None] * index[None, :]) % outer
    angles = grid.astype(jnp.float32) * angle_step
    cos_t = jnp.cos(angles)
    sin_t = jnp.sin(angles)
    table = jnp.concatenate(
        [jnp.concatenate([cos_t, -sin_t], axis=1), jnp.concatenate([sin_t, cos_t], axis=1)], axis=0
    )
    stacked = jnp.concatenate(
        [pair_re.reshape(outer, inner * width), pair_im.reshape(outer, inner * width)], axis=0
    )
    middle = jnp.dot(table, stacked, precision=precision)
    mid_re = middle[:outer]
    mid_im = middle[outer:]
    scaling = 1.0 / math.sqrt(length)
    twiddled = []
    for r in range(inner):
        part_re = mid_re[:, r * width:(r + 1) * width]
        part_im = mid_im[:, r * width:(r + 1) * width]
        if r == 0:
            twiddled.append((part_re * scaling, part_im * scaling))
            continue
        tw_angle = (r * index % length).astype(jnp.float32) * (direction * 2.0 * math.pi / length)
        tw_re = (jnp.cos(tw_angle) * scaling)[:, None]
        tw_im = (jnp.sin(tw_angle) * scaling)[:, None]
        twiddled.append((part_re * tw_re - part_im * tw_im, part_re * tw_im + part_im * tw_re))
    out_re = []
    out_im = []
    for j in range(inner):
        acc_re = None
        acc_im = None
        for r in range(inner):
            t_re, t_im = unit_times(twiddled[r][0], twiddled[r][1], direction * r * j / inner)
            acc_re = t_re if acc_re is None else acc_re + t_re
            acc_im = t_im if acc_im is None else acc_im + t_im
        out_re.append(acc_re)
        out_im.append(acc_im)
    return jnp.concatenate(out_re, axis=0), jnp.concatenate(out_im, axis=0)


def correct(field_re, field_im, measured):
    magnitude = jnp.sqrt(field_re * field_re + field_im * field_im + SOFTENING)
    factor = measured / magnitude
    return (field_re * factor - field_re, field_im * factor - field_im)


def on_device(spectrum, amplitudes, offsets, coeffs):
    led_count = lax.axis_size("led")
    row_count = lax.axis_size("row")
    led_index = lax.axis_index("led")
    row_index = lax.axis_index("row")
    size_rows = spectrum.shape[1]
    size_cols = spectrum.shape[2]
    window = amplitudes.shape[2]
    centre = window // 2
    block_rows = window // row_count
    outer_cols = window // row_count
    chunks = max(1, min(CHUNKS, size_cols // 128))
    width = size_cols // chunks
    row_shift = offsets[led_index, 0]
    col_shift = offsets[led_index, 1]
    measured = amplitudes[0]
    shape_cols = (2, block_rows, outer_cols, row_count)
    row_ids = jnp.arange(window, dtype=jnp.int32)[:, None]

    col_ids = (row_index * size_cols + jnp.arange(size_cols, dtype=jnp.int32))[None, :]
    pupil_full = pupil_at(row_ids, col_ids - col_shift, coeffs, centre)
    pupil_full = lax.optimization_barrier(pupil_full)
    pupils = [
        (pupil_full[0][:, c * width:(c + 1) * width], pupil_full[1][:, c * width:(c + 1) * width])
        for c in range(chunks)
    ]
    regions = []
    for chunk in range(chunks):
        part = spectrum[:, :, chunk * width:(chunk + 1) * width]
        regions.append(lax.all_gather(part, "led", axis=1, tiled=True))
    spreads = []
    for chunk in range(chunks):
        region = regions[chunk]
        if spreads:
            region, _ = lax.optimization_barrier((region, stacked))
        band = lax.dynamic_slice_in_dim(region, row_shift, window, 1)
        pupil_re, pupil_im = pupils[chunk]
        lit_re = pupil_re * band[0] - pupil_im * band[1]
        lit_im = pupil_re * band[1] + pupil_im * band[0]
        last = chunk == chunks - 1 and chunks > 1
        half_re, half_im = row_transform(
            lit_re, lit_im, 1.0, precision=lax.Precision.HIGH if last else HIGHEST_PRECISION
        )
        stacked = jnp.stack(
            [
                half_re.reshape(row_count, block_rows, width),
                half_im.reshape(row_count, block_rows, width),
            ],
            axis=1,
        )
        spread = lax.all_to_all(stacked, "row", split_axis=0, concat_axis=0, tiled=True)
        spreads.append(spread)
    folds = row_count * size_cols // window
    per_fold = row_count // folds
    folded = []
    for spread in spreads:
        total = spread[:per_fold]
        for f in range(1, folds):
            total = total + spread[f * per_fold:(f + 1) * per_fold]
        folded.append(total)
    window_part = (
        jnp.stack(folded, axis=1).transpose(2, 3, 0, 1, 4).reshape(2, block_rows, window)
    )
    field = transform(
        window_part.reshape(shape_cols), "ytr", "ykr", "yjk", outer_cols, row_count, 1.0
    )
    field = field.reshape(2, block_rows, window)
    diff_re, diff_im = correct(field[0], field[1], measured)
    back = transform(
        jnp.stack([diff_re, diff_im]).reshape(shape_cols),
        "ytr",
        "ykr",
        "yjk",
        outer_cols,
        row_count,
        -1.0,
    )
    back = back.reshape(2, block_rows, per_fold, chunks, width)
    gathered_all = []
    for chunk in range(chunks):
        piece = back[:, :, :, chunk, :].transpose(2, 0, 1, 3)
        piece = jnp.concatenate([piece] * folds, axis=0)
        gathered_all.append(lax.all_to_all(piece, "row", split_axis=0, concat_axis=0, tiled=True))
    results = []
    for chunk in range(chunks):
        gathered = gathered_all[chunk]
        if results:
            gathered, _ = lax.optimization_barrier((gathered, embedded))
        spec_re, spec_im = row_transform(
            gathered[:, 0].reshape(window, width), gathered[:, 1].reshape(window, width), -1.0
        )
        pupil_re, pupil_im = pupils[chunk]
        upd_re = pupil_re * spec_re + pupil_im * spec_im
        upd_im = pupil_re * spec_im - pupil_im * spec_re
        embedded = jnp.zeros((2, size_rows * led_count, width), jnp.float32)
        embedded = lax.dynamic_update_slice_in_dim(
            embedded, jnp.stack([upd_re, upd_im]), row_shift, 1
        )
        results.append(lax.psum_scatter(embedded, "led", scatter_dimension=1, tiled=True))
    out = spectrum
    for chunk in range(chunks):
        added = spectrum[:, :, chunk * width:(chunk + 1) * width] + results[chunk]
        out = lax.dynamic_update_slice_in_dim(out, added, chunk * width, 2)
    return out


def solution(mesh):
    return jax.shard_map(
        on_device,
        mesh=mesh,
        in_specs=(P(None, "led", "row"), P("led", "row", None), P(), P()),
        out_specs=P(None, "led", "row"),
        check_vma=False,
    )
```

```python
import math

import jax
import jax.numpy as jnp
from jax import lax
from jax.sharding import PartitionSpec as P


SOFTENING = 0.1
HIGHEST_PRECISION = lax.Precision.HIGHEST
CHUNKS = 4


def pupil_at(down_index, across_index, coeffs, centre):
    offset_down = down_index - centre
    offset_across = across_index - centre
    inside = offset_down * offset_down + offset_across * offset_across < centre * centre
    upper_norm = offset_down.astype(jnp.float32) * (1.0 / centre)
    lateral = offset_across.astype(jnp.float32) * (1.0 / centre)
    radial = upper_norm * upper_norm + lateral * lateral
    phases = (
        coeffs[0] * (2.0 * radial - 1.0)
        + coeffs[1] * (upper_norm * upper_norm - lateral * lateral)
        + coeffs[2] * (2.0 * upper_norm * lateral)
        + (3.0 * radial - 2.0) * (coeffs[3] * upper_norm + coeffs[4] * lateral)
        + coeffs[5] * (6.0 * radial * radial - 6.0 * radial + 1.0)
    )
    weight = jnp.where(inside, 1.0, 0.0).astype(jnp.float32)
    return (weight * jnp.cos(phases), weight * jnp.sin(phases))


def tables(outer_size, inner_size, direction):
    length = outer_size * inner_size
    angle_step = direction * 2.0 * math.pi / length
    first_index = jnp.arange(outer_size, dtype=jnp.int32)
    grid_first = first_index[:, None] * first_index[None, :] * inner_size % length
    angles_first = grid_first.astype(jnp.float32) * angle_step
    index_k = jnp.arange(outer_size, dtype=jnp.int32)[:, None, None]
    index_r = jnp.arange(inner_size, dtype=jnp.int32)[None, :, None]
    index_j = jnp.arange(inner_size, dtype=jnp.int32)[None, None, :]
    grid_second = index_r * (index_k + outer_size * index_j) % length
    angles_second = grid_second.astype(jnp.float32) * angle_step
    return (
        jnp.cos(angles_first),
        jnp.sin(angles_first),
        jnp.cos(angles_second),
        jnp.sin(angles_second),
    )


def transform(paired, inputs, middle, output, outer_size, inner_size, direction):
    first_re, first_im, second_re, second_im = tables(outer_size, inner_size, direction)
    scaling = 1.0 / math.sqrt(outer_size * inner_size)
    first_table = jnp.stack([jnp.stack([first_re, first_im]), jnp.stack([-first_im, first_re])])
    second_table = (
        jnp.stack([jnp.stack([second_re, second_im]), jnp.stack([-second_im, second_re])]) * scaling
    )
    middle_pair = jnp.einsum(
        "p" + inputs + ",pqtk->q" + middle, paired, first_table, precision=HIGHEST_PRECISION
    )
    return jnp.einsum(
        "p" + middle + ",pqkrj->q" + output, middle_pair, second_table, precision=lax.Precision.HIGH
    )


def unit_times(value_re, value_im, turn):
    eighths = round(turn * 8) % 8
    if eighths == 0:
        return value_re, value_im
    if eighths == 2:
        return -value_im, value_re
    if eighths == 4:
        return -value_re, -value_im
    if eighths == 6:
        return value_im, -value_re
    c = math.cos(2.0 * math.pi * turn)
    s = math.sin(2.0 * math.pi * turn)
    return value_re * c - value_im * s, value_re * s + value_im * c


def row_transform(pair_re, pair_im, direction, inner=4, precision=HIGHEST_PRECISION):
    length, width = pair_re.shape
    outer = length // inner
    angle_step = direction * 2.0 * math.pi / outer
    index = jnp.arange(outer, dtype=jnp.int32)
    grid = (index[:, None] * index[None, :]) % outer
    angles = grid.astype(jnp.float32) * angle_step
    cos_t = jnp.cos(angles)
    sin_t = jnp.sin(angles)
    table = jnp.concatenate(
        [jnp.concatenate([cos_t, -sin_t], axis=1), jnp.concatenate([sin_t, cos_t], axis=1)], axis=0
    )
    stacked = jnp.concatenate(
        [pair_re.reshape(outer, inner * width), pair_im.reshape(outer, inner * width)], axis=0
    )
    middle = jnp.dot(table, stacked, precision=precision)
    mid_re = middle[:outer]
    mid_im = middle[outer:]
    scaling = 1.0 / math.sqrt(length)
    twiddled = []
    for r in range(inner):
        part_re = mid_re[:, r * width:(r + 1) * width]
        part_im = mid_im[:, r * width:(r + 1) * width]
        if r == 0:
            twiddled.append((part_re * scaling, part_im * scaling))
            continue
        tw_angle = (r * index % length).astype(jnp.float32) * (direction * 2.0 * math.pi / length)
        tw_re = (jnp.cos(tw_angle) * scaling)[:, None]
        tw_im = (jnp.sin(tw_angle) * scaling)[:, None]
        twiddled.append((part_re * tw_re - part_im * tw_im, part_re * tw_im + part_im * tw_re))
    out_re = []
    out_im = []
    for j in range(inner):
        acc_re = None
        acc_im = None
        for r in range(inner):
            t_re, t_im = unit_times(twiddled[r][0], twiddled[r][1], direction * r * j / inner)
            acc_re = t_re if acc_re is None else acc_re + t_re
            acc_im = t_im if acc_im is None else acc_im + t_im
        out_re.append(acc_re)
        out_im.append(acc_im)
    return jnp.concatenate(out_re, axis=0), jnp.concatenate(out_im, axis=0)


def correct(field_re, field_im, measured):
    magnitude = jnp.sqrt(field_re * field_re + field_im * field_im + SOFTENING)
    factor = measured / magnitude
    return (field_re * factor - field_re, field_im * factor - field_im)


def on_device(spectrum, amplitudes, offsets, coeffs):
    led_count = lax.axis_size("led")
    row_count = lax.axis_size("row")
    led_index = lax.axis_index("led")
    row_index = lax.axis_index("row")
    size_rows = spectrum.shape[1]
    size_cols = spectrum.shape[2]
    window = amplitudes.shape[2]
    centre = window // 2
    block_rows = window // row_count
    outer_cols = window // row_count
    chunks = max(1, min(CHUNKS, size_cols // 128))
    width = size_cols // chunks
    row_shift = offsets[led_index, 0]
    col_shift = offsets[led_index, 1]
    measured = amplitudes[0]
    shape_cols = (2, block_rows, outer_cols, row_count)
    row_ids = jnp.arange(window, dtype=jnp.int32)[:, None]

    col_ids = (row_index * size_cols + jnp.arange(size_cols, dtype=jnp.int32))[None, :]
    pupil_full = pupil_at(row_ids, col_ids - col_shift, coeffs, centre)
    pupil_full = lax.optimization_barrier(pupil_full)
    pupils = [
        (pupil_full[0][:, c * width:(c + 1) * width], pupil_full[1][:, c * width:(c + 1) * width])
        for c in range(chunks)
    ]
    regions = []
    for chunk in range(chunks):
        part = spectrum[:, :, chunk * width:(chunk + 1) * width]
        regions.append(lax.all_gather(part, "led", axis=1, tiled=True))
    spreads = []
    for chunk in range(chunks):
        region = regions[chunk]
        if spreads:
            region, _ = lax.optimization_barrier((region, stacked))
        band = lax.dynamic_slice_in_dim(region, row_shift, window, 1)
        pupil_re, pupil_im = pupils[chunk]
        lit_re = pupil_re * band[0] - pupil_im * band[1]
        lit_im = pupil_re * band[1] + pupil_im * band[0]
        last = chunk == chunks - 1 and chunks > 1
        half_re, half_im = row_transform(
            lit_re, lit_im, 1.0, precision=lax.Precision.HIGH if last else HIGHEST_PRECISION
        )
        stacked = jnp.stack(
            [
                half_re.reshape(row_count, block_rows, width),
                half_im.reshape(row_count, block_rows, width),
            ],
            axis=1,
        )
        spread = lax.all_to_all(stacked, "row", split_axis=0, concat_axis=0, tiled=True)
        spreads.append(spread)
    folds = row_count * size_cols // window
    per_fold = row_count // folds
    folded = []
    for spread in spreads:
        total = spread[:per_fold]
        for f in range(1, folds):
            total = total + spread[f * per_fold:(f + 1) * per_fold]
        folded.append(total)
    window_part = (
        jnp.stack(folded, axis=1).transpose(2, 3, 0, 1, 4).reshape(2, block_rows, window)
    )
    field = transform(
        window_part.reshape(shape_cols), "ytr", "ykr", "yjk", outer_cols, row_count, 1.0
    )
    field = field.reshape(2, block_rows, window)
    diff_re, diff_im = correct(field[0], field[1], measured)
    back = transform(
        jnp.stack([diff_re, diff_im]).reshape(shape_cols),
        "ytr",
        "ykr",
        "yjk",
        outer_cols,
        row_count,
        -1.0,
    )
    back = back.reshape(2, block_rows, per_fold, chunks, width)
    gathered_all = []
    for chunk in range(chunks):
        piece = back[:, :, :, chunk, :].transpose(2, 0, 1, 3)
        piece = jnp.concatenate([piece] * folds, axis=0)
        gathered_all.append(lax.all_to_all(piece, "row", split_axis=0, concat_axis=0, tiled=True))
    results = []
    for chunk in range(chunks):
        gathered = gathered_all[chunk]
        if results:
            gathered, _ = lax.optimization_barrier((gathered, embedded))
        first = chunk == 0 and chunks > 1
        spec_re, spec_im = row_transform(
            gathered[:, 0].reshape(window, width),
            gathered[:, 1].reshape(window, width),
            -1.0,
            precision=lax.Precision.HIGH if first else HIGHEST_PRECISION,
        )
        pupil_re, pupil_im = pupils[chunk]
        upd_re = pupil_re * spec_re + pupil_im * spec_im
        upd_im = pupil_re * spec_im - pupil_im * spec_re
        embedded = jnp.zeros((2, size_rows * led_count, width), jnp.float32)
        embedded = lax.dynamic_update_slice_in_dim(
            embedded, jnp.stack([upd_re, upd_im]), row_shift, 1
        )
        results.append(lax.psum_scatter(embedded, "led", scatter_dimension=1, tiled=True))
    out = spectrum
    for chunk in range(chunks):
        added = spectrum[:, :, chunk * width:(chunk + 1) * width] + results[chunk]
        out = lax.dynamic_update_slice_in_dim(out, added, chunk * width, 2)
    return out


def solution(mesh):
    return jax.shard_map(
        on_device,
        mesh=mesh,
        in_specs=(P(None, "led", "row"), P("led", "row", None), P(), P()),
        out_specs=P(None, "led", "row"),
        check_vma=False,
    )
```
